128 devices in a mesh: tok: 32 (over x, y, core), tp: 4 (over z).
Axes of the slice: x: 4, y: 4, z: 4, core: 2. Of those that a mesh axis runs over, the one named last changes fastest.
Arguments:
- context: bfloat16 [16384, 1536], P('tok', 'tp'), may hold values from -6 to 6
- attn_weight: bfloat16 [1536, 1536], P('tp'), may hold values from -0.15625 to 0.15625
- residual: bfloat16 [16384, 1536], P(('tok', 'tp')), may hold values from -6 to 6
- gain_first: float32 [1536], replicated, may hold values from 0.5 to 1.5
- router: bfloat16 [1536, 40], replicated, may hold values from -46 to 46
- routes: int32 [16384, 8], P(('tok', 'tp')), may hold values from 0 to 39, as said below
- lengths: int32 [32], replicated, may hold values from 1 to 512, 14336 in all
- slot_expert: int32 [64], replicated, may hold values from 0 to 39, as said below
- w_in: bfloat16 [64, 1536, 1024], P('tok'), may hold values from -1 to 1
- w_out: bfloat16 [64, 512, 1536], P('tok'), may hold values from -1 to 1
- gain_next: float32 [1536], replicated, may hold values from 0.5 to 1.5
Outputs:
- stream_out: bfloat16 [16384, 1536], P(('tok', 'tp'))
- next_normed: bfloat16 [16384, 1536], P(('tok', 'tp'))
The draws below stay inside these ranges and needn't reach their ends.
Inputs may be any that keep to these rules, and one draw needn't show every extreme that they name: `routes`: each row names 8 different experts. In the rows of one device no expert is named by more than 30 rows, and some expert is named by exactly 30 rows. `slot_expert`: every expert is held by at least one slot; slot s lies on token shard s // 2. `lengths`: some token shard is full.
All inputs are finite; a program needn't handle non-finite values.
Results may differ from the reference program's by a relative error of at most 0.015.
Values may be sent and summed in bfloat16 or wider, within the bound.
No kernel may reach another device: no remote copies, remote signals or barrier semaphores. Data moves between devices by JAX's collectives and lax.ppermute only.
A program may use at most 128 MiB of HBM per device.

```python
import math
import jax
import jax.numpy as jnp
import numpy as np
from jax import lax

D = 1536
FF = 512
E = 40
TOPK = 8
SLOTS = 64
TOK_DEV = 512
CTX = 1536
TOKENS = 16384
ROWS_DEV = 128
MOST = 30
N_TOK = 32
N_TP = 4


def placement_table(key):
    base_key = jax.random.fold_in(key, 11)
    extra_slots = jax.random.randint(jax.random.fold_in(base_key, 1), (SLOTS - E,), 0, E, dtype=jnp.int32)
    slot_list = jnp.concatenate([jnp.arange(E, dtype=jnp.int32), extra_slots])
    shuffle = jax.random.permutation(jax.random.fold_in(base_key, 2), SLOTS)
    return slot_list[shuffle].astype(jnp.int32)


def draw_slot_expert(key, part):
    return placement_table(key)


def draw_w_in(key, part):
    mapping = placement_table(key)
    values = jnp.clip(jax.random.normal(jax.random.fold_in(key, 21), (E, D, 2 * FF), jnp.float32), -6.0, 6.0)
    experts = values * (1.5 * D ** (-0.5))
    return experts[mapping].astype(jnp.bfloat16)


def draw_w_out(key, part):
    mapping = placement_table(key)
    values = jnp.clip(jax.random.normal(jax.random.fold_in(key, 22), (E, FF, D), jnp.float32), -6.0, 6.0)
    experts = values * (1.2 * FF ** (-0.5))
    return experts[mapping].astype(jnp.bfloat16)


def draw_router(key, part):
    values = jnp.clip(jax.random.normal(jax.random.fold_in(key, 31), (D, E), jnp.float32), -6.0, 6.0)
    return (values * (0.6 * D ** (-0.5))).astype(jnp.bfloat16)


def draw_routes(key, part):
    block_count = TOKENS // ROWS_DEV
    assign = ROWS_DEV * TOPK
    full_most = assign // MOST
    full_least = max(1, full_most * 3 // 4)
    expert_bias = jax.random.randint(jax.random.fold_in(key, 41), (E,), 0, 4, dtype=jnp.int32) * 16384
    positions = jnp.arange(assign, dtype=jnp.int32)
    expert_ids = jnp.arange(E, dtype=jnp.int32)

    def one_block(block):
        block_key = jax.random.fold_in(jax.random.fold_in(key, 42), block)
        full_count = jax.random.randint(jax.random.fold_in(block_key, 1), (), full_least, full_most + 1, dtype=jnp.int32)
        remain = assign - full_count * MOST
        others = E - full_count
        share = jnp.maximum((remain + others - 1) // others, 1).astype(jnp.int32)
        rank = jnp.where(positions < full_count * MOST, positions // MOST, full_count + (positions - full_count * MOST) // share).astype(jnp.int32)
        noise = jax.random.randint(jax.random.fold_in(block_key, 2), (E,), 0, 65536, dtype=jnp.int32)
        order = jnp.argsort(-((noise + expert_bias) * E + expert_ids)).astype(jnp.int32)
        chosen = order[rank].astype(jnp.int32)
        table = chosen.reshape(TOPK, ROWS_DEV).T
        row_order = jax.random.permutation(jax.random.fold_in(block_key, 3), ROWS_DEV)
        table = table[row_order]
        offsets = jax.random.randint(jax.random.fold_in(block_key, 4), (ROWS_DEV, 1), 0, TOPK, dtype=jnp.int32)
        columns = ((jnp.arange(TOPK, dtype=jnp.int32)[None, :] + offsets) % TOPK).astype(jnp.int32)
        return jnp.take_along_axis(table, columns, axis=1)
    blocks = jax.vmap(one_block)(jnp.arange(block_count, dtype=jnp.int32))
    return blocks.reshape(TOKENS, TOPK).astype(jnp.int32)


def levels(rng, shape, pieces, smallest, high):
    def one(axis_at, shards_of):
        heights = jax.random.uniform(jax.random.fold_in(jax.random.fold_in(rng, 6), axis_at), (shards_of,), jnp.float32, smallest / len(pieces), high / len(pieces))
        return jnp.repeat(jnp.exp(heights), shape[axis_at] // shards_of).reshape((-1,) + (1,) * (len(shape) - axis_at - 1))

    level = one(*pieces[0])
    for cut in pieces[1:]:
        level = level * one(*cut)
    return level


def length_profile(count, total, limit, slope):
    weights = [(1 << 20) // math.isqrt(standing ** slope) + 1 for standing in range(2, count + 1)]
    rest, counts = total - limit - (count - 1), [1] * (count - 1)
    while rest > 0:
        free = [i for i in range(count - 1) if counts[i] < limit]
        pool, remaining = sum([weights[i] for i in free]), rest
        for i in free:
            more = min(limit - counts[i], max(1, remaining * weights[i] // pool), rest)
            counts[i] = counts[i] + more
            rest = rest - more
    return np.array([limit] + counts)


def uneven(key, amount, total, bound, skew):
    if amount == 2:
        one = jax.random.randint(key, (), max(1, total - bound), min(bound, total - 1) + 1)
        return jnp.stack([one, total - one])
    sizes = jnp.asarray(length_profile(amount, total, bound, skew), jnp.int32)
    pairs = (amount - 1) // 2
    donor, sink = sizes[1:1 + 2 * pairs:2], sizes[2:2 + 2 * pairs:2]
    slack = jnp.minimum(donor - 1, bound - sink)
    passed = jax.random.randint(jax.random.fold_in(key, 1), (pairs,), 0, 1 << 20) % (slack + 1)
    sizes = sizes.at[1:1 + 2 * pairs:2].set(donor - passed).at[2:2 + 2 * pairs:2].set(sink + passed)
    return sizes[jax.random.permutation(jax.random.fold_in(key, 2), amount)]


def bell_draw(own_key, shape, spread, most, cuts=(), held_as=jnp.bfloat16):
    array = spread * jax.random.normal(own_key, shape, jnp.float32)
    if cuts:
        array = array * levels(own_key, shape, cuts, -0.22, 0.18)
    return jnp.clip(array, -most, most).astype(held_as)


def setup_inputs(seed: int = 0) -> dict:
    key_list = jax.random.split(jax.random.key(seed), 12)
    context = bell_draw(key_list[0], (TOKENS, CTX), 1.0, 6.0, ((0, 32), (1, 4)))
    attn_weight = bell_draw(key_list[1], (CTX, D), CTX ** -0.5, 0.15625, ((0, 4),))
    residual = bell_draw(key_list[2], (TOKENS, D), 1.0, 6.0, ((0, 128),))
    gain_first = jnp.clip(1.0 + 0.1 * jax.random.normal(key_list[3], (D,), jnp.float32), 0.5, 1.5)
    router = draw_router(jax.random.fold_in(key_list[11], 71), 0)
    routes = draw_routes(jax.random.fold_in(key_list[11], 71), 0)
    lengths = uneven(key_list[6], N_TOK, TOKENS * 7 // 8, TOK_DEV, 2).astype(jnp.int32)
    slot_expert = draw_slot_expert(jax.random.fold_in(key_list[11], 71), 0)
    w_in = draw_w_in(jax.random.fold_in(key_list[11], 71), 0)
    w_out = draw_w_out(jax.random.fold_in(key_list[11], 71), 0)
    gain_next = jnp.clip(1.0 + 0.1 * jax.random.normal(key_list[10], (D,), jnp.float32), 0.5, 1.5)
    return dict(context=context, attn_weight=attn_weight, residual=residual, gain_first=gain_first, router=router, routes=routes, lengths=lengths, slot_expert=slot_expert, w_in=w_in, w_out=w_out, gain_next=gain_next)


def rms_norm(source, gain_vec):
    values = source.astype(jnp.float32)
    inverse_rms = lax.rsqrt(lax.optimization_barrier(jnp.mean(values * values, axis=-1, keepdims=True)) + 1e-06)
    return (values * inverse_rms * gain_vec.astype(jnp.float32)).astype(jnp.bfloat16)

def serve_table(slot_expert, tok_position):
    present = (slot_expert[None, :] == jnp.arange(E, dtype=jnp.int32)[:, None]).astype(jnp.int32)
    replica_count = lax.optimization_barrier(jnp.sum(present, axis=1)).astype(jnp.int32)
    replica_rank = (jnp.cumsum(present, axis=1) - 1).astype(jnp.int32)
    wanted = (tok_position % replica_count).astype(jnp.int32)
    chosen_slot = (present == 1) & (replica_rank == wanted[:, None])
    slot_ids = jnp.arange(SLOTS, dtype=jnp.int32)[None, :]
    return lax.optimization_barrier(jnp.sum(jnp.where(chosen_slot, slot_ids, 0), axis=1)).astype(jnp.int32)

def reference(context, attn_weight, residual, gain_first, router, routes, lengths, slot_expert, w_in, w_out, gain_next):
    attn_out = jnp.dot(context, attn_weight, preferred_element_type=jnp.float32)
    stream = (residual.astype(jnp.float32) + attn_out).astype(jnp.bfloat16)
    normed = rms_norm(stream, gain_first)
    logits = jnp.dot(normed, router, preferred_element_type=jnp.float32)
    scores = jnp.take_along_axis(logits, routes, axis=1)
    gate_probs = jax.nn.softmax(scores, axis=-1)
    row_index = jnp.arange(TOKENS, dtype=jnp.int32)
    shard_index = (row_index // TOK_DEV).astype(jnp.int32)
    live_rows = row_index % TOK_DEV < lengths[shard_index]
    all_tables = jax.vmap(lambda tok_position: serve_table(slot_expert, tok_position))(jnp.arange(N_TOK, dtype=jnp.int32))
    slot_of = all_tables[shard_index[:, None], routes]
    weight_flat = jnp.where(live_rows[:, None], gate_probs, jnp.float32(0.0)).reshape(-1)
    slot_flat = jnp.where(live_rows[:, None], slot_of, -1).reshape(-1).astype(jnp.int32)
    row_of = (jnp.arange(TOKENS * TOPK, dtype=jnp.int32) // TOPK).astype(jnp.int32)
    capacity = N_TOK * N_TP * MOST

    def per_slot(expert_sum, slot_index):
        is_match = slot_flat == slot_index
        slot_rank = (jnp.cumsum(is_match.astype(jnp.int32)) - 1).astype(jnp.int32)
        target = jnp.where(is_match, slot_rank, capacity).astype(jnp.int32)
        rows_idx = jnp.zeros((capacity,), jnp.int32).at[target].set(row_of, mode='drop')
        row_weights = jnp.zeros((capacity,), jnp.float32).at[target].set(weight_flat, mode='drop')
        picked = normed[rows_idx]
        hidden = jnp.dot(picked, w_in[slot_index], preferred_element_type=jnp.float32)
        activated = (jax.nn.silu(hidden[:, :FF]) * hidden[:, FF:]).astype(jnp.bfloat16)
        expert_out = jnp.dot(activated, w_out[slot_index], preferred_element_type=jnp.float32).astype(jnp.bfloat16)
        expert_sum = expert_sum.at[rows_idx].add(expert_out.astype(jnp.float32) * row_weights[:, None])
        return (expert_sum, None)
    expert_sum, _ = lax.scan(per_slot, jnp.zeros((TOKENS, D), jnp.float32), jnp.arange(SLOTS, dtype=jnp.int32))
    stream_out = (stream.astype(jnp.float32) + expert_sum).astype(jnp.bfloat16)
    next_normed = rms_norm(stream_out, gain_next)
    return (stream_out, next_normed)
```

```python
import jax
import jax.numpy as jnp
from jax import lax
from jax.sharding import PartitionSpec as P

E = 40
TOPK = 8
MOST = 30
DEPTH = 32


def rms_norm(source, gain_vec):
    values = source.astype(jnp.float32)
    inverse_rms = lax.rsqrt(jnp.mean(values * values, axis=-1, keepdims=True) + 1e-06)
    return (values * inverse_rms * gain_vec).astype(jnp.bfloat16)


def serve_slots(slot_expert, tok_position):
    slot_total = slot_expert.shape[0]
    present = (slot_expert[None, :] == jnp.arange(E, dtype=jnp.int32)[:, None]).astype(jnp.int32)
    replica_count = jnp.sum(present, axis=1)
    replica_rank = jnp.cumsum(present, axis=1) - 1
    wanted = tok_position % replica_count
    chosen_slot = (present == 1) & (replica_rank == wanted[:, None])
    slot_ids = jnp.arange(slot_total, dtype=jnp.int32)[None, :]
    return jnp.sum(jnp.where(chosen_slot, slot_ids, 0), axis=1)


def shards(
    context,
    attn_weight,
    residual,
    gain_first,
    router,
    routes,
    lengths,
    slot_expert,
    w_in,
    w_out,
    gain_next,
):
    row_count = residual.shape[0]
    width = residual.shape[1]
    hidden_units = w_out.shape[1]
    local_slots = w_in.shape[0]
    tok_rank = lax.axis_index("tok")
    tp_rank = lax.axis_index("tp")
    tok_total = lax.axis_size("tok")
    slot_total = slot_expert.shape[0]
    capacity = slot_total * DEPTH
    attn_out = lax.psum_scatter(
        jnp.dot(context, attn_weight, preferred_element_type=jnp.float32).astype(jnp.bfloat16),
        "tp",
        scatter_dimension=0,
        tiled=True,
    ).astype(jnp.float32)
    stream = (residual.astype(jnp.float32) + attn_out).astype(jnp.bfloat16)
    normed = rms_norm(stream, gain_first)
    logits = jnp.dot(normed, router, preferred_element_type=jnp.float32)
    chooser = routes[:, :, None] == jnp.arange(E, dtype=jnp.int32)[None, None, :]
    scores = jnp.sum(jnp.where(chooser, logits[:, None, :], jnp.float32(0.0)), axis=-1)
    gate_probs = jax.nn.softmax(scores, axis=-1)
    length_cap = jnp.sum(
        jnp.where(jnp.arange(lengths.shape[0], dtype=jnp.int32) == tok_rank, lengths, 0)
    )
    live_rows = tp_rank * row_count + jnp.arange(row_count, dtype=jnp.int32) < length_cap
    serving = serve_slots(slot_expert, tok_rank)
    slot_of = jnp.sum(jnp.where(chooser, serving[None, None, :], 0), axis=-1)
    named = (jnp.any(chooser, axis=1) & live_rows[:, None]).astype(jnp.bfloat16)
    row_ids = jnp.arange(row_count, dtype=jnp.int32)
    before = (row_ids[None, :] < row_ids[:, None]).astype(jnp.bfloat16)
    earlier = jnp.dot(before, named, preferred_element_type=jnp.float32).astype(jnp.int32)
    position = jnp.sum(jnp.where(chooser, earlier[:, None, :], 0), axis=-1)
    target = jnp.where(live_rows[:, None], slot_of * DEPTH + position, capacity)
    picks = target[:, :, None] == jnp.arange(capacity, dtype=jnp.int32)[None, None, :]
    dispatch = jnp.any(picks, axis=1).astype(jnp.bfloat16)
    outgoing = lax.dot_general(
        dispatch, normed, (((0,), (0,)), ((), ())), preferred_element_type=jnp.float32
    ).astype(jnp.bfloat16)
    outgoing = outgoing.reshape(tok_total, local_slots * DEPTH, width)
    arrived = lax.all_to_all(outgoing, "tok", split_axis=0, concat_axis=0, tiled=True)
    arrived = arrived.reshape(tok_total, local_slots, DEPTH, width)
    hidden = jnp.einsum("nsmd,sdf->nsmf", arrived, w_in, preferred_element_type=jnp.float32)
    activated = (jax.nn.silu(hidden[..., :hidden_units]) * hidden[..., hidden_units:]).astype(
        jnp.bfloat16
    )
    computed = jnp.einsum(
        "nsmf,sfd->nsmd", activated, w_out, preferred_element_type=jnp.float32
    ).astype(jnp.bfloat16)
    computed = computed.reshape(tok_total, local_slots * DEPTH, width)
    returned = lax.all_to_all(computed, "tok", split_axis=0, concat_axis=0, tiled=True)
    returned = returned.reshape(capacity, width)
    gate_live = jnp.where(live_rows[:, None], gate_probs, jnp.float32(0.0))
    combine = jnp.sum(jnp.where(picks, gate_live[:, :, None], jnp.float32(0.0)), axis=1)
    combine_hi = combine.astype(jnp.bfloat16)
    combine_lo = (combine - combine_hi.astype(jnp.float32)).astype(jnp.bfloat16)
    expert_sum = jnp.dot(combine_hi, returned, preferred_element_type=jnp.float32) + jnp.dot(
        combine_lo, returned, preferred_element_type=jnp.float32
    )
    stream_out = (stream.astype(jnp.float32) + expert_sum).astype(jnp.bfloat16)
    next_normed = rms_norm(stream_out, gain_next)
    return (stream_out, next_normed)


def solution(mesh):
    return jax.shard_map(
        shards,
        mesh=mesh,
        in_specs=(
            P("tok", "tp"),
            P("tp", None),
            P(("tok", "tp"), None),
            P(),
            P(),
            P(("tok", "tp"), None),
            P(),
            P(),
            P("tok", None, None),
            P("tok", None, None),
            P(),
        ),
        out_specs=(P(("tok", "tp"), None), P(("tok", "tp"), None)),
        check_vma=False,
    )
```

```python
import jax
import jax.numpy as jnp
from jax import lax
from jax.sharding import PartitionSpec as P

E = 40
TOPK = 8
MOST = 30
DEPTH = 32


def rms_norm(source, gain_vec):
    values = source.astype(jnp.float32)
    inverse_rms = lax.rsqrt(jnp.mean(values * values, axis=-1, keepdims=True) + 1e-06)
    return (values * inverse_rms * gain_vec).astype(jnp.bfloat16)


def serve_slots(slot_expert, tok_position):
    slot_total = slot_expert.shape[0]
    present = (slot_expert[None, :] == jnp.arange(E, dtype=jnp.int32)[:, None]).astype(jnp.int32)
    replica_count = jnp.sum(present, axis=1)
    replica_rank = jnp.cumsum(present, axis=1) - 1
    wanted = tok_position % replica_count
    chosen_slot = (present == 1) & (replica_rank == wanted[:, None])
    slot_ids = jnp.arange(slot_total, dtype=jnp.int32)[None, :]
    return jnp.sum(jnp.where(chosen_slot, slot_ids, 0), axis=1)


def shards(
    context,
    attn_weight,
    residual,
    gain_first,
    router,
    routes,
    lengths,
    slot_expert,
    w_in,
    w_out,
    gain_next,
):
    row_count = residual.shape[0]
    width = residual.shape[1]
    hidden_units = w_out.shape[1]
    local_slots = w_in.shape[0]
    tok_rank = lax.axis_index("tok")
    tp_rank = lax.axis_index("tp")
    tok_total = lax.axis_size("tok")
    slot_total = slot_expert.shape[0]
    capacity = slot_total * DEPTH
    tp_total = lax.axis_size("tp")
    partial = jnp.dot(context, attn_weight, preferred_element_type=jnp.float32).astype(jnp.bfloat16)
    blocks = partial.reshape(tp_total, row_count, width)
    attn_out = blocks[tp_rank].astype(jnp.float32)
    for shift in range(1, tp_total):
        sent = blocks[(tp_rank + shift) % tp_total]
        pairs = [(j, (j + shift) % tp_total) for j in range(tp_total)]
        attn_out = attn_out + lax.ppermute(sent, "tp", pairs).astype(jnp.float32)
    stream = (residual.astype(jnp.float32) + attn_out).astype(jnp.bfloat16)
    normed = rms_norm(stream, gain_first)
    logits = jnp.dot(normed, router, preferred_element_type=jnp.float32)
    chooser = routes[:, :, None] == jnp.arange(E, dtype=jnp.int32)[None, None, :]
    scores = jnp.sum(jnp.where(chooser, logits[:, None, :], jnp.float32(0.0)), axis=-1)
    gate_probs = jax.nn.softmax(scores, axis=-1)
    length_cap = jnp.sum(
        jnp.where(jnp.arange(lengths.shape[0], dtype=jnp.int32) == tok_rank, lengths, 0)
    )
    live_rows = tp_rank * row_count + jnp.arange(row_count, dtype=jnp.int32) < length_cap
    serving = serve_slots(slot_expert, tok_rank)
    slot_of = jnp.sum(jnp.where(chooser, serving[None, None, :], 0), axis=-1)
    named = (jnp.any(chooser, axis=1) & live_rows[:, None]).astype(jnp.bfloat16)
    row_ids = jnp.arange(row_count, dtype=jnp.int32)
    before = (row_ids[None, :] < row_ids[:, None]).astype(jnp.bfloat16)
    earlier = jnp.dot(before, named, preferred_element_type=jnp.float32).astype(jnp.int32)
    position = jnp.sum(jnp.where(chooser, earlier[:, None, :], 0), axis=-1)
    target = jnp.where(live_rows[:, None], slot_of * DEPTH + position, capacity)
    picks = target[:, :, None] == jnp.arange(capacity, dtype=jnp.int32)[None, None, :]
    dispatch = jnp.any(picks, axis=1).astype(jnp.bfloat16)
    outgoing = lax.dot_general(
        dispatch, normed, (((0,), (0,)), ((), ())), preferred_element_type=jnp.float32
    ).astype(jnp.bfloat16)
    outgoing = outgoing.reshape(tok_total, local_slots * DEPTH, width)
    arrived = lax.all_to_all(outgoing, "tok", split_axis=0, concat_axis=0, tiled=True)
    arrived = arrived.reshape(tok_total, local_slots, DEPTH, width)
    hidden = jnp.einsum("nsmd,sdf->nsmf", arrived, w_in, preferred_element_type=jnp.float32)
    activated = (jax.nn.silu(hidden[..., :hidden_units]) * hidden[..., hidden_units:]).astype(
        jnp.bfloat16
    )
    computed = jnp.einsum(
        "nsmf,sfd->nsmd", activated, w_out, preferred_element_type=jnp.float32
    ).astype(jnp.bfloat16)
    computed = computed.reshape(tok_total, local_slots * DEPTH, width)
    returned = lax.all_to_all(computed, "tok", split_axis=0, concat_axis=0, tiled=True)
    returned = returned.reshape(capacity, width)
    gate_live = jnp.where(live_rows[:, None], gate_probs, jnp.float32(0.0))
    combine = jnp.sum(jnp.where(picks, gate_live[:, :, None], jnp.float32(0.0)), axis=1)
    combine_hi = combine.astype(jnp.bfloat16)
    combine_lo = (combine - combine_hi.astype(jnp.float32)).astype(jnp.bfloat16)
    expert_sum = jnp.dot(combine_hi, returned, preferred_element_type=jnp.float32) + jnp.dot(
        combine_lo, returned, preferred_element_type=jnp.float32
    )
    stream_out = (stream.astype(jnp.float32) + expert_sum).astype(jnp.bfloat16)
    next_normed = rms_norm(stream_out, gain_next)
    return (stream_out, next_normed)


def solution(mesh):
    return jax.shard_map(
        shards,
        mesh=mesh,
        in_specs=(
            P("tok", "tp"),
            P("tp", None),
            P(("tok", "tp"), None),
            P(),
            P(),
            P(("tok", "tp"), None),
            P(),
            P(),
            P("tok", None, None),
            P("tok", None, None),
            P(),
        ),
        out_specs=(P(("tok", "tp"), None), P(("tok", "tp"), None)),
        check_vma=False,
    )
```

```python
import jax
import jax.numpy as jnp
from jax import lax
from jax.sharding import PartitionSpec as P

E = 40
TOPK = 8
MOST = 30
DEPTH = 32


def rms_norm(source, gain_vec):
    values = source.astype(jnp.float32)
    inverse_rms = lax.rsqrt(jnp.mean(values * values, axis=-1, keepdims=True) + 1e-06)
    return (values * inverse_rms * gain_vec).astype(jnp.bfloat16)


def serve_slots(slot_expert, tok_position):
    slot_total = slot_expert.shape[0]
    present = (slot_expert[None, :] == jnp.arange(E, dtype=jnp.int32)[:, None]).astype(jnp.int32)
    replica_count = jnp.sum(present, axis=1)
    replica_rank = jnp.cumsum(present, axis=1) - 1
    wanted = tok_position % replica_count
    chosen_slot = (present == 1) & (replica_rank == wanted[:, None])
    slot_ids = jnp.arange(slot_total, dtype=jnp.int32)[None, :]
    return jnp.sum(jnp.where(chosen_slot, slot_ids, 0), axis=1)


def shards(
    context,
    attn_weight,
    residual,
    gain_first,
    router,
    routes,
    lengths,
    slot_expert,
    w_in,
    w_out,
    gain_next,
):
    row_count = residual.shape[0]
    width = residual.shape[1]
    hidden_units = w_out.shape[1]
    local_slots = w_in.shape[0]
    tok_rank = lax.axis_index("tok")
    tp_rank = lax.axis_index("tp")
    tok_total = lax.axis_size("tok")
    slot_total = slot_expert.shape[0]
    capacity = slot_total * DEPTH
    tp_total = lax.axis_size("tp")
    partial = jnp.dot(context, attn_weight, preferred_element_type=jnp.float32).astype(jnp.bfloat16)
    blocks = partial.reshape(tp_total, row_count, width)
    attn_out = blocks[tp_rank].astype(jnp.float32)
    for shift in range(1, tp_total):
        sent = blocks[(tp_rank + shift) % tp_total]
        pairs = [(j, (j + shift) % tp_total) for j in range(tp_total)]
        attn_out = attn_out + lax.ppermute(sent, "tp", pairs).astype(jnp.float32)
    stream = (residual.astype(jnp.float32) + attn_out).astype(jnp.bfloat16)
    normed = rms_norm(stream, gain_first)
    logits = jnp.dot(normed, router, preferred_element_type=jnp.float32)
    chooser = routes[:, :, None] == jnp.arange(E, dtype=jnp.int32)[None, None, :]
    scores = jnp.sum(jnp.where(chooser, logits[:, None, :], jnp.float32(0.0)), axis=-1)
    gate_probs = jax.nn.softmax(scores, axis=-1)
    length_cap = jnp.sum(
        jnp.where(jnp.arange(lengths.shape[0], dtype=jnp.int32) == tok_rank, lengths, 0)
    )
    live_rows = tp_rank * row_count + jnp.arange(row_count, dtype=jnp.int32) < length_cap
    serving = serve_slots(slot_expert, tok_rank)
    slot_of = jnp.sum(jnp.where(chooser, serving[None, None, :], 0), axis=-1)
    named = (jnp.any(chooser, axis=1) & live_rows[:, None]).astype(jnp.bfloat16)
    row_ids = jnp.arange(row_count, dtype=jnp.int32)
    before = (row_ids[None, :] < row_ids[:, None]).astype(jnp.bfloat16)
    earlier = jnp.dot(before, named, preferred_element_type=jnp.float32).astype(jnp.int32)
    position = jnp.sum(jnp.where(chooser, earlier[:, None, :], 0), axis=-1)
    target = jnp.where(live_rows[:, None], slot_of * DEPTH + position, capacity)
    gate_live = jnp.where(live_rows[:, None], gate_probs, jnp.float32(0.0))
    column = jnp.arange(tok_total * DEPTH, dtype=jnp.int32)
    expert_sum = jnp.zeros((row_count, width), jnp.float32)
    for local in range(local_slots):
        slot_cols = (column // DEPTH) * (local_slots * DEPTH) + local * DEPTH + column % DEPTH
        picks = target[:, :, None] == slot_cols[None, None, :]
        dispatch = jnp.any(picks, axis=1).astype(jnp.bfloat16)
        outgoing = lax.dot_general(
            dispatch, normed, (((0,), (0,)), ((), ())), preferred_element_type=jnp.float32
        ).astype(jnp.bfloat16)
        outgoing = outgoing.reshape(tok_total, DEPTH, width)
        arrived = lax.all_to_all(outgoing, "tok", split_axis=0, concat_axis=0, tiled=True)
        arrived = arrived.reshape(tok_total * DEPTH, width)
        hidden = jnp.dot(arrived, w_in[local], preferred_element_type=jnp.float32)
        activated = (
            jax.nn.silu(hidden[:, :hidden_units]) * hidden[:, hidden_units:]
        ).astype(jnp.bfloat16)
        computed = jnp.dot(activated, w_out[local], preferred_element_type=jnp.float32).astype(
            jnp.bfloat16
        )
        computed = computed.reshape(tok_total, DEPTH, width)
        returned = lax.all_to_all(computed, "tok", split_axis=0, concat_axis=0, tiled=True)
        returned = returned.reshape(tok_total * DEPTH, width)
        combine = jnp.sum(jnp.where(picks, gate_live[:, :, None], jnp.float32(0.0)), axis=1)
        combine_hi = combine.astype(jnp.bfloat16)
        combine_lo = (combine - combine_hi.astype(jnp.float32)).astype(jnp.bfloat16)
        expert_sum = expert_sum + (
            jnp.dot(combine_hi, returned, preferred_element_type=jnp.float32)
            + jnp.dot(combine_lo, returned, preferred_element_type=jnp.float32)
        )
    stream_out = (stream.astype(jnp.float32) + expert_sum).astype(jnp.bfloat16)
    next_normed = rms_norm(stream_out, gain_next)
    return (stream_out, next_normed)


def solution(mesh):
    return jax.shard_map(
        shards,
        mesh=mesh,
        in_specs=(
            P("tok", "tp"),
            P("tp", None),
            P(("tok", "tp"), None),
            P(),
            P(),
            P(("tok", "tp"), None),
            P(),
            P(),
            P("tok", None, None),
            P("tok", None, None),
            P(),
        ),
        out_specs=(P(("tok", "tp"), None), P(("tok", "tp"), None)),
        check_vma=False,
    )
```

```python
import jax
import jax.numpy as jnp
from jax import lax
from jax.sharding import PartitionSpec as P

E = 40
TOPK = 8
MOST = 30
DEPTH = 32


def rms_norm(source, gain_vec):
    values = source.astype(jnp.float32)
    inverse_rms = lax.rsqrt(jnp.mean(values * values, axis=-1, keepdims=True) + 1e-06)
    return (values * inverse_rms * gain_vec).astype(jnp.bfloat16)


def serve_slots(slot_expert, tok_position):
    slot_total = slot_expert.shape[0]
    present = (slot_expert[None, :] == jnp.arange(E, dtype=jnp.int32)[:, None]).astype(jnp.int32)
    replica_count = jnp.sum(present, axis=1)
    replica_rank = jnp.cumsum(present, axis=1) - 1
    wanted = tok_position % replica_count
    chosen_slot = (present == 1) & (replica_rank == wanted[:, None])
    slot_ids = jnp.arange(slot_total, dtype=jnp.int32)[None, :]
    return jnp.sum(jnp.where(chosen_slot, slot_ids, 0), axis=1)


def shards(
    context,
    attn_weight,
    residual,
    gain_first,
    router,
    routes,
    lengths,
    slot_expert,
    w_in,
    w_out,
    gain_next,
):
    row_count = residual.shape[0]
    width = residual.shape[1]
    hidden_units = w_out.shape[1]
    local_slots = w_in.shape[0]
    tok_rank = lax.axis_index("tok")
    tp_rank = lax.axis_index("tp")
    tok_total = lax.axis_size("tok")
    slot_total = slot_expert.shape[0]
    capacity = slot_total * DEPTH
    tp_total = lax.axis_size("tp")
    partial = jnp.dot(context, attn_weight, preferred_element_type=jnp.float32).astype(jnp.bfloat16)
    blocks = partial.reshape(tp_total, row_count, width)
    attn_out = blocks[tp_rank].astype(jnp.float32)
    for shift in range(1, tp_total):
        sent = blocks[(tp_rank + shift) % tp_total]
        pairs = [(j, (j + shift) % tp_total) for j in range(tp_total)]
        attn_out = attn_out + lax.ppermute(sent, "tp", pairs).astype(jnp.float32)
    stream = (residual.astype(jnp.float32) + attn_out).astype(jnp.bfloat16)
    normed = rms_norm(stream, gain_first)
    logits = jnp.dot(normed, router, preferred_element_type=jnp.float32)
    chooser = routes[:, :, None] == jnp.arange(E, dtype=jnp.int32)[None, None, :]
    scores = jnp.sum(jnp.where(chooser, logits[:, None, :], jnp.float32(0.0)), axis=-1)
    gate_probs = jax.nn.softmax(scores, axis=-1)
    length_cap = jnp.sum(
        jnp.where(jnp.arange(lengths.shape[0], dtype=jnp.int32) == tok_rank, lengths, 0)
    )
    live_rows = tp_rank * row_count + jnp.arange(row_count, dtype=jnp.int32) < length_cap
    serving = serve_slots(slot_expert, tok_rank)
    slot_of = jnp.sum(jnp.where(chooser, serving[None, None, :], 0), axis=-1)
    named = (jnp.any(chooser, axis=1) & live_rows[:, None]).astype(jnp.bfloat16)
    row_ids = jnp.arange(row_count, dtype=jnp.int32)
    before = (row_ids[None, :] < row_ids[:, None]).astype(jnp.bfloat16)
    earlier = jnp.dot(before, named, preferred_element_type=jnp.float32).astype(jnp.int32)
    position = jnp.sum(jnp.where(chooser, earlier[:, None, :], 0), axis=-1)
    shift_of = (slot_of // local_slots - tok_rank) % tok_total
    chunk = local_slots * DEPTH
    local_of = slot_of % local_slots
    target = jnp.where(
        live_rows[:, None], shift_of * chunk + local_of * DEPTH + position, capacity
    )
    picks = target[:, :, None] == jnp.arange(capacity, dtype=jnp.int32)[None, None, :]
    dispatch = jnp.any(picks, axis=1).astype(jnp.bfloat16)
    outgoing = lax.dot_general(
        dispatch, normed, (((0,), (0,)), ((), ())), preferred_element_type=jnp.float32
    ).astype(jnp.bfloat16)
    outgoing = outgoing.reshape(tok_total, chunk, width)
    pieces = [outgoing[0]]
    for shift in range(1, tok_total):
        pairs = [(j, (j + shift) % tok_total) for j in range(tok_total)]
        pieces.append(lax.ppermute(outgoing[shift], "tok", pairs))
    arrived = jnp.stack(pieces).reshape(tok_total, local_slots, DEPTH, width)
    hidden = jnp.einsum("nsmd,sdf->nsmf", arrived, w_in, preferred_element_type=jnp.float32)
    activated = (jax.nn.silu(hidden[..., :hidden_units]) * hidden[..., hidden_units:]).astype(
        jnp.bfloat16
    )
    computed = jnp.einsum(
        "nsmf,sfd->nsmd", activated, w_out, preferred_element_type=jnp.float32
    ).astype(jnp.bfloat16)
    computed = computed.reshape(tok_total, chunk, width)
    pieces = [computed[0]]
    for shift in range(1, tok_total):
        pairs = [(j, (j - shift) % tok_total) for j in range(tok_total)]
        pieces.append(lax.ppermute(computed[shift], "tok", pairs))
    returned = jnp.stack(pieces).reshape(capacity, width)
    gate_live = jnp.where(live_rows[:, None], gate_probs, jnp.float32(0.0))
    combine = jnp.sum(jnp.where(picks, gate_live[:, :, None], jnp.float32(0.0)), axis=1)
    combine_hi = combine.astype(jnp.bfloat16)
    combine_lo = (combine - combine_hi.astype(jnp.float32)).astype(jnp.bfloat16)
    expert_sum = jnp.dot(combine_hi, returned, preferred_element_type=jnp.float32) + jnp.dot(
        combine_lo, returned, preferred_element_type=jnp.float32
    )
    stream_out = (stream.astype(jnp.float32) + expert_sum).astype(jnp.bfloat16)
    next_normed = rms_norm(stream_out, gain_next)
    return (stream_out, next_normed)


def solution(mesh):
    return jax.shard_map(
        shards,
        mesh=mesh,
        in_specs=(
            P("tok", "tp"),
            P("tp", None),
            P(("tok", "tp"), None),
            P(),
            P(),
            P(("tok", "tp"), None),
            P(),
            P(),
            P("tok", None, None),
            P("tok", None, None),
            P(),
        ),
        out_specs=(P(("tok", "tp"), None), P(("tok", "tp"), None)),
        check_vma=False,
    )
```

```python
import jax
import jax.numpy as jnp
from jax import lax
from jax.sharding import PartitionSpec as P

E = 40
TOPK = 8
MOST = 30
DEPTH = 32


def rms_norm(source, gain_vec):
    values = source.astype(jnp.float32)
    inverse_rms = lax.rsqrt(jnp.mean(values * values, axis=-1, keepdims=True) + 1e-06)
    return (values * inverse_rms * gain_vec).astype(jnp.bfloat16)


def serve_slots(slot_expert, tok_position):
    slot_total = slot_expert.shape[0]
    present = (slot_expert[None, :] == jnp.arange(E, dtype=jnp.int32)[:, None]).astype(jnp.int32)
    replica_count = jnp.sum(present, axis=1)
    replica_rank = jnp.cumsum(present, axis=1) - 1
    wanted = tok_position % replica_count
    chosen_slot = (present == 1) & (replica_rank == wanted[:, None])
    slot_ids = jnp.arange(slot_total, dtype=jnp.int32)[None, :]
    return jnp.sum(jnp.where(chosen_slot, slot_ids, 0), axis=1)


def shards(
    context,
    attn_weight,
    residual,
    gain_first,
    router,
    routes,
    lengths,
    slot_expert,
    w_in,
    w_out,
    gain_next,
):
    row_count = residual.shape[0]
    width = residual.shape[1]
    hidden_units = w_out.shape[1]
    local_slots = w_in.shape[0]
    tok_rank = lax.axis_index("tok")
    tp_rank = lax.axis_index("tp")
    tok_total = lax.axis_size("tok")
    slot_total = slot_expert.shape[0]
    capacity = slot_total * DEPTH
    tp_total = lax.axis_size("tp")
    half = row_count // 2

    def block_for(shift):
        rows = lax.dynamic_slice_in_dim(context, ((tp_rank + shift) % tp_total) * row_count, row_count)
        return jnp.dot(rows, attn_weight, preferred_element_type=jnp.float32).astype(jnp.bfloat16)

    up = [(j, (j + 1) % tp_total) for j in range(tp_total)]
    down = [(j, (j - 1) % tp_total) for j in range(tp_total)]
    far = block_for(2)
    from_below = lax.ppermute(jnp.concatenate([block_for(1), far[:half]]), "tp", up)
    from_above = lax.ppermute(jnp.concatenate([block_for(3), far[half:]]), "tp", down)
    relayed_up = lax.ppermute(from_below[row_count:], "tp", up)
    relayed_down = lax.ppermute(from_above[row_count:], "tp", down)
    attn_out = (
        block_for(0).astype(jnp.float32)
        + from_below[:row_count].astype(jnp.float32)
        + from_above[:row_count].astype(jnp.float32)
        + jnp.concatenate([relayed_up, relayed_down]).astype(jnp.float32)
    )
    stream = (residual.astype(jnp.float32) + attn_out).astype(jnp.bfloat16)
    normed = rms_norm(stream, gain_first)
    logits = jnp.dot(normed, router, preferred_element_type=jnp.float32)
    chooser = routes[:, :, None] == jnp.arange(E, dtype=jnp.int32)[None, None, :]
    scores = jnp.sum(jnp.where(chooser, logits[:, None, :], jnp.float32(0.0)), axis=-1)
    gate_probs = jax.nn.softmax(scores, axis=-1)
    length_cap = jnp.sum(
        jnp.where(jnp.arange(lengths.shape[0], dtype=jnp.int32) == tok_rank, lengths, 0)
    )
    live_rows = tp_rank * row_count + jnp.arange(row_count, dtype=jnp.int32) < length_cap
    serving = serve_slots(slot_expert, tok_rank)
    slot_of = jnp.sum(jnp.where(chooser, serving[None, None, :], 0), axis=-1)
    named = (jnp.any(chooser, axis=1) & live_rows[:, None]).astype(jnp.bfloat16)
    row_ids = jnp.arange(row_count, dtype=jnp.int32)
    before = (row_ids[None, :] < row_ids[:, None]).astype(jnp.bfloat16)
    earlier = jnp.dot(before, named, preferred_element_type=jnp.float32).astype(jnp.int32)
    position = jnp.sum(jnp.where(chooser, earlier[:, None, :], 0), axis=-1)
    target = jnp.where(live_rows[:, None], slot_of * DEPTH + position, capacity)
    gate_live = jnp.where(live_rows[:, None], gate_probs, jnp.float32(0.0))
    column = jnp.arange(tok_total * DEPTH, dtype=jnp.int32)
    expert_sum = jnp.zeros((row_count, width), jnp.float32)
    for local in range(local_slots):
        slot_cols = (column // DEPTH) * (local_slots * DEPTH) + local * DEPTH + column % DEPTH
        picks = target[:, :, None] == slot_cols[None, None, :]
        dispatch = jnp.any(picks, axis=1).astype(jnp.bfloat16)
        outgoing = lax.dot_general(
            dispatch, normed, (((0,), (0,)), ((), ())), preferred_element_type=jnp.float32
        ).astype(jnp.bfloat16)
        outgoing = outgoing.reshape(tok_total, DEPTH, width)
        arrived = lax.all_to_all(outgoing, "tok", split_axis=0, concat_axis=0, tiled=True)
        arrived = arrived.reshape(tok_total * DEPTH, width)
        hidden = jnp.dot(arrived, w_in[local], preferred_element_type=jnp.float32)
        activated = (
            jax.nn.silu(hidden[:, :hidden_units]) * hidden[:, hidden_units:]
        ).astype(jnp.bfloat16)
        computed = jnp.dot(activated, w_out[local], preferred_element_type=jnp.float32).astype(
            jnp.bfloat16
        )
        computed = computed.reshape(tok_total, DEPTH, width)
        returned = lax.all_to_all(computed, "tok", split_axis=0, concat_axis=0, tiled=True)
        returned = returned.reshape(tok_total * DEPTH, width)
        combine = jnp.sum(jnp.where(picks, gate_live[:, :, None], jnp.float32(0.0)), axis=1)
        combine_hi = combine.astype(jnp.bfloat16)
        combine_lo = (combine - combine_hi.astype(jnp.float32)).astype(jnp.bfloat16)
        expert_sum = expert_sum + (
            jnp.dot(combine_hi, returned, preferred_element_type=jnp.float32)
            + jnp.dot(combine_lo, returned, preferred_element_type=jnp.float32)
        )
    stream_out = (stream.astype(jnp.float32) + expert_sum).astype(jnp.bfloat16)
    next_normed = rms_norm(stream_out, gain_next)
    return (stream_out, next_normed)


def solution(mesh):
    return jax.shard_map(
        shards,
        mesh=mesh,
        in_specs=(
            P("tok", "tp"),
            P("tp", None),
            P(("tok", "tp"), None),
            P(),
            P(),
            P(("tok", "tp"), None),
            P(),
            P(),
            P("tok", None, None),
            P("tok", None, None),
            P(),
        ),
        out_specs=(P(("tok", "tp"), None), P(("tok", "tp"), None)),
        check_vma=False,
    )
```

```python
import jax
import jax.numpy as jnp
from jax import lax
from jax.sharding import PartitionSpec as P

E = 40
TOPK = 8
MOST = 30
DEPTH = 32


def rms_norm(source, gain_vec):
    values = source.astype(jnp.float32)
    inverse_rms = lax.rsqrt(jnp.mean(values * values, axis=-1, keepdims=True) + 1e-06)
    return (values * inverse_rms * gain_vec).astype(jnp.bfloat16)


def serve_slots(slot_expert, tok_position):
    slot_total = slot_expert.shape[0]
    present = (slot_expert[None, :] == jnp.arange(E, dtype=jnp.int32)[:, None]).astype(jnp.int32)
    replica_count = jnp.sum(present, axis=1)
    replica_rank = jnp.cumsum(present, axis=1) - 1
    wanted = tok_position % replica_count
    chosen_slot = (present == 1) & (replica_rank == wanted[:, None])
    slot_ids = jnp.arange(slot_total, dtype=jnp.int32)[None, :]
    return jnp.sum(jnp.where(chosen_slot, slot_ids, 0), axis=1)


def shards(
    context,
    attn_weight,
    residual,
    gain_first,
    router,
    routes,
    lengths,
    slot_expert,
    w_in,
    w_out,
    gain_next,
):
    row_count = residual.shape[0]
    width = residual.shape[1]
    hidden_units = w_out.shape[1]
    local_slots = w_in.shape[0]
    tok_rank = lax.axis_index("tok")
    tp_rank = lax.axis_index("tp")
    tok_total = lax.axis_size("tok")
    slot_total = slot_expert.shape[0]
    capacity = slot_total * DEPTH
    tp_total = lax.axis_size("tp")
    partial = jnp.dot(context, attn_weight, preferred_element_type=jnp.float32).astype(jnp.bfloat16)
    blocks = partial.reshape(tp_total, row_count, width)
    attn_out = blocks[tp_rank].astype(jnp.float32)
    for shift in range(1, tp_total):
        sent = blocks[(tp_rank + shift) % tp_total]
        pairs = [(j, (j + shift) % tp_total) for j in range(tp_total)]
        attn_out = attn_out + lax.ppermute(sent, "tp", pairs).astype(jnp.float32)
    stream = (residual.astype(jnp.float32) + attn_out).astype(jnp.bfloat16)
    normed = rms_norm(stream, gain_first)
    logits = jnp.dot(normed, router, preferred_element_type=jnp.float32)
    chooser = routes[:, :, None] == jnp.arange(E, dtype=jnp.int32)[None, None, :]
    scores = jnp.sum(jnp.where(chooser, logits[:, None, :], jnp.float32(0.0)), axis=-1)
    gate_probs = jax.nn.softmax(scores, axis=-1)
    length_cap = jnp.sum(
        jnp.where(jnp.arange(lengths.shape[0], dtype=jnp.int32) == tok_rank, lengths, 0)
    )
    live_rows = tp_rank * row_count + jnp.arange(row_count, dtype=jnp.int32) < length_cap
    serving = serve_slots(slot_expert, tok_rank)
    slot_of = jnp.sum(jnp.where(chooser, serving[None, None, :], 0), axis=-1)
    named = (jnp.any(chooser, axis=1) & live_rows[:, None]).astype(jnp.bfloat16)
    row_ids = jnp.arange(row_count, dtype=jnp.int32)
    before = (row_ids[None, :] < row_ids[:, None]).astype(jnp.bfloat16)
    earlier = jnp.dot(before, named, preferred_element_type=jnp.float32).astype(jnp.int32)
    position = jnp.sum(jnp.where(chooser, earlier[:, None, :], 0), axis=-1)
    target = jnp.where(live_rows[:, None], slot_of * DEPTH + position, capacity)
    gate_live = jnp.where(live_rows[:, None], gate_probs, jnp.float32(0.0))
    picks = target[:, :, None] == jnp.arange(capacity, dtype=jnp.int32)[None, None, :]
    dispatch = jnp.any(picks, axis=1).astype(jnp.bfloat16)
    outgoing = lax.dot_general(
        dispatch, normed, (((0,), (0,)), ((), ())), preferred_element_type=jnp.float32
    ).astype(jnp.bfloat16)
    outgoing = outgoing.reshape(tok_total, local_slots * DEPTH, width)
    arrived = lax.all_to_all(outgoing, "tok", split_axis=0, concat_axis=0, tiled=True)
    arrived = arrived.reshape(tok_total, local_slots, DEPTH, width)
    combine_all = jnp.sum(jnp.where(picks, gate_live[:, :, None], jnp.float32(0.0)), axis=1)
    combine_all = combine_all.reshape(row_count, tok_total, local_slots, DEPTH)
    expert_sum = jnp.zeros((row_count, width), jnp.float32)
    for local in range(local_slots):
        rows_in = arrived[:, local].reshape(tok_total * DEPTH, width)
        hidden = jnp.dot(rows_in, w_in[local], preferred_element_type=jnp.float32)
        activated = (
            jax.nn.silu(hidden[:, :hidden_units]) * hidden[:, hidden_units:]
        ).astype(jnp.bfloat16)
        computed = jnp.dot(activated, w_out[local], preferred_element_type=jnp.float32).astype(
            jnp.bfloat16
        )
        computed = computed.reshape(tok_total, DEPTH, width)
        returned = lax.all_to_all(computed, "tok", split_axis=0, concat_axis=0, tiled=True)
        returned = returned.reshape(tok_total * DEPTH, width)
        combine = combine_all[:, :, local].reshape(row_count, tok_total * DEPTH)
        combine_hi = combine.astype(jnp.bfloat16)
        combine_lo = (combine - combine_hi.astype(jnp.float32)).astype(jnp.bfloat16)
        expert_sum = expert_sum + (
            jnp.dot(combine_hi, returned, preferred_element_type=jnp.float32)
            + jnp.dot(combine_lo, returned, preferred_element_type=jnp.float32)
        )
    stream_out = (stream.astype(jnp.float32) + expert_sum).astype(jnp.bfloat16)
    next_normed = rms_norm(stream_out, gain_next)
    return (stream_out, next_normed)


def solution(mesh):
    return jax.shard_map(
        shards,
        mesh=mesh,
        in_specs=(
            P("tok", "tp"),
            P("tp", None),
            P(("tok", "tp"), None),
            P(),
            P(),
            P(("tok", "tp"), None),
            P(),
            P(),
            P("tok", None, None),
            P("tok", None, None),
            P(),
        ),
        out_specs=(P(("tok", "tp"), None), P(("tok", "tp"), None)),
        check_vma=False,
    )
```

```python
import jax
import jax.numpy as jnp
from jax import lax
from jax.sharding import PartitionSpec as P

E = 40
TOPK = 8
MOST = 30
DEPTH = 32


def rms_norm(source, gain_vec):
    values = source.astype(jnp.float32)
    inverse_rms = lax.rsqrt(jnp.mean(values * values, axis=-1, keepdims=True) + 1e-06)
    return (values * inverse_rms * gain_vec).astype(jnp.bfloat16)


def serve_slots(slot_expert, tok_position):
    slot_total = slot_expert.shape[0]
    present = (slot_expert[None, :] == jnp.arange(E, dtype=jnp.int32)[:, None]).astype(jnp.int32)
    replica_count = jnp.sum(present, axis=1)
    replica_rank = jnp.cumsum(present, axis=1) - 1
    wanted = tok_position % replica_count
    chosen_slot = (present == 1) & (replica_rank == wanted[:, None])
    slot_ids = jnp.arange(slot_total, dtype=jnp.int32)[None, :]
    return jnp.sum(jnp.where(chosen_slot, slot_ids, 0), axis=1)


def shards(
    context,
    attn_weight,
    residual,
    gain_first,
    router,
    routes,
    lengths,
    slot_expert,
    w_in,
    w_out,
    gain_next,
):
    row_count = residual.shape[0]
    width = residual.shape[1]
    hidden_units = w_out.shape[1]
    local_slots = w_in.shape[0]
    tok_rank = lax.axis_index("tok")
    tp_rank = lax.axis_index("tp")
    tok_total = lax.axis_size("tok")
    slot_total = slot_expert.shape[0]
    capacity = slot_total * DEPTH
    tp_total = lax.axis_size("tp")
    partial = jnp.dot(context, attn_weight, preferred_element_type=jnp.float32).astype(jnp.bfloat16)
    blocks = partial.reshape(tp_total, row_count, width)
    attn_out = blocks[tp_rank].astype(jnp.float32)
    for shift in range(1, tp_total):
        sent = blocks[(tp_rank + shift) % tp_total]
        pairs = [(j, (j + shift) % tp_total) for j in range(tp_total)]
        attn_out = attn_out + lax.ppermute(sent, "tp", pairs).astype(jnp.float32)
    stream = (residual.astype(jnp.float32) + attn_out).astype(jnp.bfloat16)
    normed = rms_norm(stream, gain_first)
    logits = jnp.dot(normed, router, preferred_element_type=jnp.float32)
    chooser = routes[:, :, None] == jnp.arange(E, dtype=jnp.int32)[None, None, :]
    scores = jnp.sum(jnp.where(chooser, logits[:, None, :], jnp.float32(0.0)), axis=-1)
    gate_probs = jax.nn.softmax(scores, axis=-1)
    length_cap = jnp.sum(
        jnp.where(jnp.arange(lengths.shape[0], dtype=jnp.int32) == tok_rank, lengths, 0)
    )
    live_rows = tp_rank * row_count + jnp.arange(row_count, dtype=jnp.int32) < length_cap
    serving = serve_slots(slot_expert, tok_rank)
    slot_of = jnp.sum(jnp.where(chooser, serving[None, None, :], 0), axis=-1)
    named = (jnp.any(chooser, axis=1) & live_rows[:, None]).astype(jnp.bfloat16)
    row_ids = jnp.arange(row_count, dtype=jnp.int32)
    before = (row_ids[None, :] < row_ids[:, None]).astype(jnp.bfloat16)
    earlier = jnp.dot(before, named, preferred_element_type=jnp.float32).astype(jnp.int32)
    position = jnp.sum(jnp.where(chooser, earlier[:, None, :], 0), axis=-1)
    target = jnp.where(live_rows[:, None], slot_of * DEPTH + position, capacity)
    gate_live = jnp.where(live_rows[:, None], gate_probs, jnp.float32(0.0))
    picks = target[:, :, None] == jnp.arange(capacity, dtype=jnp.int32)[None, None, :]
    dispatch = jnp.any(picks, axis=1).astype(jnp.bfloat16)
    outgoing = lax.dot_general(
        dispatch, normed, (((0,), (0,)), ((), ())), preferred_element_type=jnp.float32
    ).astype(jnp.bfloat16)
    outgoing = outgoing.reshape(tok_total, local_slots * DEPTH, width)
    arrived = lax.all_to_all(outgoing, "tok", split_axis=0, concat_axis=0, tiled=True)
    arrived = arrived.reshape(tok_total, local_slots, DEPTH, width)
    combine_all = jnp.sum(jnp.where(picks, gate_live[:, :, None], jnp.float32(0.0)), axis=1)
    combine_all = combine_all.reshape(row_count, tok_total, local_slots, DEPTH)
    expert_sum = jnp.zeros((row_count, width), jnp.float32)
    for local in range(local_slots):
        rows_in = arrived[:, local].reshape(tok_total * DEPTH, width)
        hidden = jnp.dot(rows_in, w_in[local], preferred_element_type=jnp.float32)
        activated = (
            jax.nn.silu(hidden[:, :hidden_units]) * hidden[:, hidden_units:]
        ).astype(jnp.bfloat16)
        computed = jnp.dot(activated, w_out[local], preferred_element_type=jnp.float32).astype(
            jnp.bfloat16
        )
        computed = computed.reshape(tok_total, DEPTH, width)
        returned = lax.all_to_all(computed, "tok", split_axis=0, concat_axis=0, tiled=True)
        returned = returned.reshape(tok_total * DEPTH, width)
        combine = combine_all[:, :, local].reshape(row_count, tok_total * DEPTH)
        combine_hi = combine.astype(jnp.bfloat16)
        combine_lo = (combine - combine_hi.astype(jnp.float32)).astype(jnp.bfloat16)
        both = jnp.dot(
            jnp.concatenate([combine_hi, combine_lo]), returned, preferred_element_type=jnp.float32
        )
        expert_sum = expert_sum + (both[:row_count] + both[row_count:])
    stream_out = (stream.astype(jnp.float32) + expert_sum).astype(jnp.bfloat16)
    next_normed = rms_norm(stream_out, gain_next)
    return (stream_out, next_normed)


def solution(mesh):
    return jax.shard_map(
        shards,
        mesh=mesh,
        in_specs=(
            P("tok", "tp"),
            P("tp", None),
            P(("tok", "tp"), None),
            P(),
            P(),
            P(("tok", "tp"), None),
            P(),
            P(),
            P("tok", None, None),
            P("tok", None, None),
            P(),
        ),
        out_specs=(P(("tok", "tp"), None), P(("tok", "tp"), None)),
        check_vma=False,
    )
```

```python
import jax
import jax.numpy as jnp
from jax import lax
from jax.sharding import PartitionSpec as P

E = 40
TOPK = 8
MOST = 30
DEPTH = 32


def rms_norm(source, gain_vec):
    values = source.astype(jnp.float32)
    inverse_rms = lax.rsqrt(jnp.mean(values * values, axis=-1, keepdims=True) + 1e-06)
    return (values * inverse_rms * gain_vec).astype(jnp.bfloat16)


def serve_slots(slot_expert, tok_position):
    slot_total = slot_expert.shape[0]
    present = (slot_expert[None, :] == jnp.arange(E, dtype=jnp.int32)[:, None]).astype(jnp.int32)
    replica_count = jnp.sum(present, axis=1)
    replica_rank = jnp.cumsum(present, axis=1) - 1
    wanted = tok_position % replica_count
    chosen_slot = (present == 1) & (replica_rank == wanted[:, None])
    slot_ids = jnp.arange(slot_total, dtype=jnp.int32)[None, :]
    return jnp.sum(jnp.where(chosen_slot, slot_ids, 0), axis=1)


def shards(
    context,
    attn_weight,
    residual,
    gain_first,
    router,
    routes,
    lengths,
    slot_expert,
    w_in,
    w_out,
    gain_next,
):
    row_count = residual.shape[0]
    width = residual.shape[1]
    hidden_units = w_out.shape[1]
    local_slots = w_in.shape[0]
    tok_rank = lax.axis_index("tok")
    tp_rank = lax.axis_index("tp")
    tok_total = lax.axis_size("tok")
    slot_total = slot_expert.shape[0]
    capacity = slot_total * DEPTH
    tp_total = lax.axis_size("tp")

    def block_for(shift):
        start = ((tp_rank + shift) % tp_total) * row_count
        rows = lax.dynamic_slice_in_dim(context, start, row_count)
        return jnp.dot(rows, attn_weight, preferred_element_type=jnp.float32).astype(jnp.bfloat16)

    received = {}
    for shift in [tp_total // 2] + [k for k in range(1, tp_total) if k != tp_total // 2]:
        pairs = [(j, (j + shift) % tp_total) for j in range(tp_total)]
        received[shift] = lax.ppermute(block_for(shift), "tp", pairs)
    attn_out = block_for(0).astype(jnp.float32)
    for shift in range(1, tp_total):
        attn_out = attn_out + received[shift].astype(jnp.float32)
    stream = (residual.astype(jnp.float32) + attn_out).astype(jnp.bfloat16)
    normed = rms_norm(stream, gain_first)
    logits = jnp.dot(normed, router, preferred_element_type=jnp.float32)
    chooser = routes[:, :, None] == jnp.arange(E, dtype=jnp.int32)[None, None, :]
    scores = jnp.sum(jnp.where(chooser, logits[:, None, :], jnp.float32(0.0)), axis=-1)
    gate_probs = jax.nn.softmax(scores, axis=-1)
    length_cap = jnp.sum(
        jnp.where(jnp.arange(lengths.shape[0], dtype=jnp.int32) == tok_rank, lengths, 0)
    )
    live_rows = tp_rank * row_count + jnp.arange(row_count, dtype=jnp.int32) < length_cap
    serving = serve_slots(slot_expert, tok_rank)
    slot_of = jnp.sum(jnp.where(chooser, serving[None, None, :], 0), axis=-1)
    named = (jnp.any(chooser, axis=1) & live_rows[:, None]).astype(jnp.bfloat16)
    row_ids = jnp.arange(row_count, dtype=jnp.int32)
    before = (row_ids[None, :] < row_ids[:, None]).astype(jnp.bfloat16)
    earlier = jnp.dot(before, named, preferred_element_type=jnp.float32).astype(jnp.int32)
    position = jnp.sum(jnp.where(chooser, earlier[:, None, :], 0), axis=-1)
    target = jnp.where(live_rows[:, None], slot_of * DEPTH + position, capacity)
    gate_live = jnp.where(live_rows[:, None], gate_probs, jnp.float32(0.0))
    picks = target[:, :, None] == jnp.arange(capacity, dtype=jnp.int32)[None, None, :]
    dispatch = jnp.any(picks, axis=1).astype(jnp.bfloat16)
    outgoing = lax.dot_general(
        dispatch, normed, (((0,), (0,)), ((), ())), preferred_element_type=jnp.float32
    ).astype(jnp.bfloat16)
    outgoing = outgoing.reshape(tok_total, local_slots * DEPTH, width)
    arrived = lax.all_to_all(outgoing, "tok", split_axis=0, concat_axis=0, tiled=True)
    arrived = arrived.reshape(tok_total, local_slots, DEPTH, width)
    combine_all = jnp.sum(jnp.where(picks, gate_live[:, :, None], jnp.float32(0.0)), axis=1)
    combine_all = combine_all.reshape(row_count, tok_total, local_slots, DEPTH)
    expert_sum = jnp.zeros((row_count, width), jnp.float32)
    for local in range(local_slots):
        rows_in = arrived[:, local].reshape(tok_total * DEPTH, width)
        hidden = jnp.dot(rows_in, w_in[local], preferred_element_type=jnp.float32)
        activated = (
            jax.nn.silu(hidden[:, :hidden_units]) * hidden[:, hidden_units:]
        ).astype(jnp.bfloat16)
        computed = jnp.dot(activated, w_out[local], preferred_element_type=jnp.float32).astype(
            jnp.bfloat16
        )
        computed = computed.reshape(tok_total, DEPTH, width)
        returned = lax.all_to_all(computed, "tok", split_axis=0, concat_axis=0, tiled=True)
        returned = returned.reshape(tok_total * DEPTH, width)
        combine = combine_all[:, :, local].reshape(row_count, tok_total * DEPTH)
        combine_hi = combine.astype(jnp.bfloat16)
        combine_lo = (combine - combine_hi.astype(jnp.float32)).astype(jnp.bfloat16)
        both = jnp.dot(
            jnp.concatenate([combine_hi, combine_lo]), returned, preferred_element_type=jnp.float32
        )
        expert_sum = expert_sum + (both[:row_count] + both[row_count:])
    stream_out = (stream.astype(jnp.float32) + expert_sum).astype(jnp.bfloat16)
    next_normed = rms_norm(stream_out, gain_next)
    return (stream_out, next_normed)


def solution(mesh):
    return jax.shard_map(
        shards,
        mesh=mesh,
        in_specs=(
            P("tok", "tp"),
            P("tp", None),
            P(("tok", "tp"), None),
            P(),
            P(),
            P(("tok", "tp"), None),
            P(),
            P(),
            P("tok", None, None),
            P("tok", None, None),
            P(),
        ),
        out_specs=(P(("tok", "tp"), None), P(("tok", "tp"), None)),
        check_vma=False,
    )
```

```python
import jax
import jax.numpy as jnp
from jax import lax
from jax.sharding import PartitionSpec as P

E = 40
TOPK = 8
MOST = 30
DEPTH = 32


def rms_norm(source, gain_vec):
    values = source.astype(jnp.float32)
    inverse_rms = lax.rsqrt(jnp.mean(values * values, axis=-1, keepdims=True) + 1e-06)
    return (values * inverse_rms * gain_vec).astype(jnp.bfloat16)


def serve_slots(slot_expert, tok_position):
    slot_total = slot_expert.shape[0]
    present = (slot_expert[None, :] == jnp.arange(E, dtype=jnp.int32)[:, None]).astype(jnp.int32)
    replica_count = jnp.sum(present, axis=1)
    replica_rank = jnp.cumsum(present, axis=1) - 1
    wanted = tok_position % replica_count
    chosen_slot = (present == 1) & (replica_rank == wanted[:, None])
    slot_ids = jnp.arange(slot_total, dtype=jnp.int32)[None, :]
    return jnp.sum(jnp.where(chosen_slot, slot_ids, 0), axis=1)


def shards(
    context,
    attn_weight,
    residual,
    gain_first,
    router,
    routes,
    lengths,
    slot_expert,
    w_in,
    w_out,
    gain_next,
):
    row_count = residual.shape[0]
    width = residual.shape[1]
    hidden_units = w_out.shape[1]
    local_slots = w_in.shape[0]
    tok_rank = lax.axis_index("tok")
    tp_rank = lax.axis_index("tp")
    tok_total = lax.axis_size("tok")
    slot_total = slot_expert.shape[0]
    capacity = slot_total * DEPTH
    tp_total = lax.axis_size("tp")

    def block_for(shift):
        start = ((tp_rank + shift) % tp_total) * row_count
        rows = lax.dynamic_slice_in_dim(context, start, row_count)
        return jnp.dot(rows, attn_weight, preferred_element_type=jnp.float32).astype(jnp.bfloat16)

    received = {}
    for shift in [tp_total // 2] + [k for k in range(1, tp_total) if k != tp_total // 2]:
        pairs = [(j, (j + shift) % tp_total) for j in range(tp_total)]
        received[shift] = lax.ppermute(block_for(shift), "tp", pairs)
    attn_out = block_for(0).astype(jnp.float32)
    for shift in range(1, tp_total):
        attn_out = attn_out + received[shift].astype(jnp.float32)
    stream = (residual.astype(jnp.float32) + attn_out).astype(jnp.bfloat16)
    normed = rms_norm(stream, gain_first)
    logits = jnp.dot(normed, router, preferred_element_type=jnp.float32)
    chooser = routes[:, :, None] == jnp.arange(E, dtype=jnp.int32)[None, None, :]
    scores = jnp.sum(jnp.where(chooser, logits[:, None, :], jnp.float32(0.0)), axis=-1)
    gate_probs = jax.nn.softmax(scores, axis=-1)
    length_cap = jnp.sum(
        jnp.where(jnp.arange(lengths.shape[0], dtype=jnp.int32) == tok_rank, lengths, 0)
    )
    live_rows = tp_rank * row_count + jnp.arange(row_count, dtype=jnp.int32) < length_cap
    serving = serve_slots(slot_expert, tok_rank)
    slot_of = jnp.sum(jnp.where(chooser, serving[None, None, :], 0), axis=-1)
    named = (jnp.any(chooser, axis=1) & live_rows[:, None]).astype(jnp.bfloat16)
    row_ids = jnp.arange(row_count, dtype=jnp.int32)
    before = (row_ids[None, :] < row_ids[:, None]).astype(jnp.bfloat16)
    earlier = jnp.dot(before, named, preferred_element_type=jnp.float32).astype(jnp.int32)
    position = jnp.sum(jnp.where(chooser, earlier[:, None, :], 0), axis=-1)
    target = jnp.where(live_rows[:, None], slot_of * DEPTH + position, capacity)
    gate_live = jnp.where(live_rows[:, None], gate_probs, jnp.float32(0.0))
    picks = target[:, :, None] == jnp.arange(capacity, dtype=jnp.int32)[None, None, :]
    dispatch = jnp.any(picks, axis=1).astype(jnp.bfloat16)
    outgoing = lax.dot_general(
        dispatch, stream, (((0,), (0,)), ((), ())), preferred_element_type=jnp.float32
    ).astype(jnp.bfloat16)
    outgoing = outgoing.reshape(tok_total, local_slots * DEPTH, width)
    arrived = lax.all_to_all(outgoing, "tok", split_axis=0, concat_axis=0, tiled=True)
    arrived = arrived.reshape(tok_total, local_slots, DEPTH, width)
    combine_all = jnp.sum(jnp.where(picks, gate_live[:, :, None], jnp.float32(0.0)), axis=1)
    combine_all = combine_all.reshape(row_count, tok_total, local_slots, DEPTH)
    expert_sum = jnp.zeros((row_count, width), jnp.float32)
    for local in range(local_slots):
        rows_in = rms_norm(arrived[:, local].reshape(tok_total * DEPTH, width), gain_first)
        hidden = jnp.dot(rows_in, w_in[local], preferred_element_type=jnp.float32)
        activated = (
            jax.nn.silu(hidden[:, :hidden_units]) * hidden[:, hidden_units:]
        ).astype(jnp.bfloat16)
        computed = jnp.dot(activated, w_out[local], preferred_element_type=jnp.float32).astype(
            jnp.bfloat16
        )
        computed = computed.reshape(tok_total, DEPTH, width)
        returned = lax.all_to_all(computed, "tok", split_axis=0, concat_axis=0, tiled=True)
        returned = returned.reshape(tok_total * DEPTH, width)
        combine = combine_all[:, :, local].reshape(row_count, tok_total * DEPTH)
        combine_hi = combine.astype(jnp.bfloat16)
        combine_lo = (combine - combine_hi.astype(jnp.float32)).astype(jnp.bfloat16)
        both = jnp.dot(
            jnp.concatenate([combine_hi, combine_lo]), returned, preferred_element_type=jnp.float32
        )
        expert_sum = expert_sum + (both[:row_count] + both[row_count:])
    stream_out = (stream.astype(jnp.float32) + expert_sum).astype(jnp.bfloat16)
    next_normed = rms_norm(stream_out, gain_next)
    return (stream_out, next_normed)


def solution(mesh):
    return jax.shard_map(
        shards,
        mesh=mesh,
        in_specs=(
            P("tok", "tp"),
            P("tp", None),
            P(("tok", "tp"), None),
            P(),
            P(),
            P(("tok", "tp"), None),
            P(),
            P(),
            P("tok", None, None),
            P("tok", None, None),
            P(),
        ),
        out_specs=(P(("tok", "tp"), None), P(("tok", "tp"), None)),
        check_vma=False,
    )
```

```python
import jax
import jax.numpy as jnp
from jax import lax
from jax.sharding import PartitionSpec as P

E = 40
TOPK = 8
MOST = 30
DEPTH = 32


def rms_norm(source, gain_vec):
    values = source.astype(jnp.float32)
    inverse_rms = lax.rsqrt(jnp.mean(values * values, axis=-1, keepdims=True) + 1e-06)
    return (values * inverse_rms * gain_vec).astype(jnp.bfloat16)


def serve_slots(slot_expert, tok_position):
    slot_total = slot_expert.shape[0]
    present = (slot_expert[None, :] == jnp.arange(E, dtype=jnp.int32)[:, None]).astype(jnp.int32)
    replica_count = jnp.sum(present, axis=1)
    replica_rank = jnp.cumsum(present, axis=1) - 1
    wanted = tok_position % replica_count
    chosen_slot = (present == 1) & (replica_rank == wanted[:, None])
    slot_ids = jnp.arange(slot_total, dtype=jnp.int32)[None, :]
    return jnp.sum(jnp.where(chosen_slot, slot_ids, 0), axis=1)


def shards(
    context,
    attn_weight,
    residual,
    gain_first,
    router,
    routes,
    lengths,
    slot_expert,
    w_in,
    w_out,
    gain_next,
):
    row_count = residual.shape[0]
    width = residual.shape[1]
    hidden_units = w_out.shape[1]
    local_slots = w_in.shape[0]
    tok_rank = lax.axis_index("tok")
    tp_rank = lax.axis_index("tp")
    tok_total = lax.axis_size("tok")
    slot_total = slot_expert.shape[0]
    capacity = slot_total * DEPTH
    tp_total = lax.axis_size("tp")

    def block_for(shift):
        start = ((tp_rank + shift) % tp_total) * row_count
        rows = lax.dynamic_slice_in_dim(context, start, row_count)
        return jnp.dot(rows, attn_weight, preferred_element_type=jnp.float32).astype(jnp.bfloat16)

    received = {}
    for shift in [tp_total // 2] + [k for k in range(1, tp_total) if k != tp_total // 2]:
        pairs = [(j, (j + shift) % tp_total) for j in range(tp_total)]
        received[shift] = lax.ppermute(block_for(shift), "tp", pairs)
    attn_out = block_for(0).astype(jnp.float32)
    for shift in range(1, tp_total):
        attn_out = attn_out + received[shift].astype(jnp.float32)
    stream = (residual.astype(jnp.float32) + attn_out).astype(jnp.bfloat16)
    normed = rms_norm(stream, gain_first)
    logits = jnp.dot(normed, router, preferred_element_type=jnp.float32)
    chooser = routes[:, :, None] == jnp.arange(E, dtype=jnp.int32)[None, None, :]
    scores = jnp.sum(jnp.where(chooser, logits[:, None, :], jnp.float32(0.0)), axis=-1)
    gate_probs = jax.nn.softmax(scores, axis=-1)
    length_cap = jnp.sum(
        jnp.where(jnp.arange(lengths.shape[0], dtype=jnp.int32) == tok_rank, lengths, 0)
    )
    live_rows = tp_rank * row_count + jnp.arange(row_count, dtype=jnp.int32) < length_cap
    serving = serve_slots(slot_expert, tok_rank)
    slot_of = jnp.sum(jnp.where(chooser, serving[None, None, :], 0), axis=-1)
    named = (jnp.any(chooser, axis=1) & live_rows[:, None]).astype(jnp.bfloat16)
    row_ids = jnp.arange(row_count, dtype=jnp.int32)
    before = (row_ids[None, :] < row_ids[:, None]).astype(jnp.bfloat16)
    earlier = jnp.dot(before, named, preferred_element_type=jnp.float32).astype(jnp.int32)
    position = jnp.sum(jnp.where(chooser, earlier[:, None, :], 0), axis=-1)
    target = jnp.where(live_rows[:, None], slot_of * DEPTH + position, capacity)
    gate_live = jnp.where(live_rows[:, None], gate_probs, jnp.float32(0.0))
    picks = target[:, :, None] == jnp.arange(capacity, dtype=jnp.int32)[None, None, :]
    dispatch = jnp.any(picks, axis=1).astype(jnp.bfloat16)
    outgoing = lax.dot_general(
        dispatch, normed, (((0,), (0,)), ((), ())), preferred_element_type=jnp.float32
    ).astype(jnp.bfloat16)
    outgoing = outgoing.reshape(tok_total, local_slots * DEPTH, width)
    arrived = lax.all_to_all(outgoing, "tok", split_axis=0, concat_axis=0, tiled=True)
    arrived = arrived.reshape(tok_total, local_slots, DEPTH, width)
    combine_all = jnp.sum(jnp.where(picks, gate_live[:, :, None], jnp.float32(0.0)), axis=1)
    combine_all = combine_all.reshape(row_count, tok_total, local_slots, DEPTH)
    expert_sum = jnp.zeros((row_count, width), jnp.float32)
    for local in range(local_slots):
        rows_in = arrived[:, local].reshape(tok_total * DEPTH, width)
        hidden = jnp.dot(rows_in, w_in[local], preferred_element_type=jnp.float32)
        activated = (
            jax.nn.silu(hidden[:, :hidden_units]) * hidden[:, hidden_units:]
        ).astype(jnp.bfloat16)
        computed = jnp.dot(activated, w_out[local], preferred_element_type=jnp.float32).astype(
            jnp.bfloat16
        )
        computed = computed.reshape(tok_total, DEPTH, width)
        arrived, computed = lax.optimization_barrier((arrived, computed))
        returned = lax.all_to_all(computed, "tok", split_axis=0, concat_axis=0, tiled=True)
        returned = returned.reshape(tok_total * DEPTH, width)
        combine = combine_all[:, :, local].reshape(row_count, tok_total * DEPTH)
        combine_hi = combine.astype(jnp.bfloat16)
        combine_lo = (combine - combine_hi.astype(jnp.float32)).astype(jnp.bfloat16)
        both = jnp.dot(
            jnp.concatenate([combine_hi, combine_lo]), returned, preferred_element_type=jnp.float32
        )
        expert_sum = expert_sum + (both[:row_count] + both[row_count:])
    stream_out = (stream.astype(jnp.float32) + expert_sum).astype(jnp.bfloat16)
    next_normed = rms_norm(stream_out, gain_next)
    return (stream_out, next_normed)


def solution(mesh):
    return jax.shard_map(
        shards,
        mesh=mesh,
        in_specs=(
            P("tok", "tp"),
            P("tp", None),
            P(("tok", "tp"), None),
            P(),
            P(),
            P(("tok", "tp"), None),
            P(),
            P(),
            P("tok", None, None),
            P("tok", None, None),
            P(),
        ),
        out_specs=(P(("tok", "tp"), None), P(("tok", "tp"), None)),
        check_vma=False,
    )
```

```python
import jax
import jax.numpy as jnp
from jax import lax
from jax.sharding import PartitionSpec as P

E = 40
TOPK = 8
MOST = 30
DEPTH = 32


def rms_norm(source, gain_vec):
    values = source.astype(jnp.float32)
    inverse_rms = lax.rsqrt(jnp.mean(values * values, axis=-1, keepdims=True) + 1e-06)
    return (values * inverse_rms * gain_vec).astype(jnp.bfloat16)


def serve_slots(slot_expert, tok_position):
    slot_total = slot_expert.shape[0]
    present = (slot_expert[None, :] == jnp.arange(E, dtype=jnp.int32)[:, None]).astype(jnp.int32)
    replica_count = jnp.sum(present, axis=1)
    replica_rank = jnp.cumsum(present, axis=1) - 1
    wanted = tok_position % replica_count
    chosen_slot = (present == 1) & (replica_rank == wanted[:, None])
    slot_ids = jnp.arange(slot_total, dtype=jnp.int32)[None, :]
    return jnp.sum(jnp.where(chosen_slot, slot_ids, 0), axis=1)


def shards(
    context,
    attn_weight,
    residual,
    gain_first,
    router,
    routes,
    lengths,
    slot_expert,
    w_in,
    w_out,
    gain_next,
):
    row_count = residual.shape[0]
    width = residual.shape[1]
    hidden_units = w_out.shape[1]
    local_slots = w_in.shape[0]
    tok_rank = lax.axis_index("tok")
    tp_rank = lax.axis_index("tp")
    tok_total = lax.axis_size("tok")
    slot_total = slot_expert.shape[0]
    capacity = slot_total * DEPTH
    tp_total = lax.axis_size("tp")

    def block_for(shift):
        start = ((tp_rank + shift) % tp_total) * row_count
        rows = lax.dynamic_slice_in_dim(context, start, row_count)
        return jnp.dot(rows, attn_weight, preferred_element_type=jnp.float32).astype(jnp.bfloat16)

    received = {}
    for shift in [tp_total // 2] + [k for k in range(1, tp_total) if k != tp_total // 2]:
        pairs = [(j, (j + shift) % tp_total) for j in range(tp_total)]
        received[shift] = lax.ppermute(block_for(shift), "tp", pairs)
    attn_out = block_for(0).astype(jnp.float32)
    for shift in range(1, tp_total):
        attn_out = attn_out + received[shift].astype(jnp.float32)
    stream = (residual.astype(jnp.float32) + attn_out).astype(jnp.bfloat16)
    normed = rms_norm(stream, gain_first)
    logits = jnp.dot(normed, router, preferred_element_type=jnp.float32)
    chooser = routes[:, :, None] == jnp.arange(E, dtype=jnp.int32)[None, None, :]
    scores = jnp.sum(jnp.where(chooser, logits[:, None, :], jnp.float32(0.0)), axis=-1)
    gate_probs = jax.nn.softmax(scores, axis=-1)
    length_cap = jnp.sum(
        jnp.where(jnp.arange(lengths.shape[0], dtype=jnp.int32) == tok_rank, lengths, 0)
    )
    live_rows = tp_rank * row_count + jnp.arange(row_count, dtype=jnp.int32) < length_cap
    serving = serve_slots(slot_expert, tok_rank)
    slot_of = jnp.sum(jnp.where(chooser, serving[None, None, :], 0), axis=-1)
    named = (jnp.any(chooser, axis=1) & live_rows[:, None]).astype(jnp.bfloat16)
    row_ids = jnp.arange(row_count, dtype=jnp.int32)
    before = (row_ids[None, :] < row_ids[:, None]).astype(jnp.bfloat16)
    earlier = jnp.dot(before, named, preferred_element_type=jnp.float32).astype(jnp.int32)
    position = jnp.sum(jnp.where(chooser, earlier[:, None, :], 0), axis=-1)
    target = jnp.where(live_rows[:, None], slot_of * DEPTH + position, capacity)
    gate_live = jnp.where(live_rows[:, None], gate_probs, jnp.float32(0.0))
    picks = target[:, :, None] == jnp.arange(capacity, dtype=jnp.int32)[None, None, :]
    dispatch = jnp.any(picks, axis=1).astype(jnp.bfloat16)
    outgoing = lax.dot_general(
        dispatch, normed, (((0,), (0,)), ((), ())), preferred_element_type=jnp.float32
    ).astype(jnp.bfloat16)
    outgoing = outgoing.reshape(tok_total, local_slots * DEPTH, width)
    arrived = lax.all_to_all(outgoing, "tok", split_axis=0, concat_axis=0, tiled=True)
    arrived = arrived.reshape(tok_total, local_slots, DEPTH, width)
    combine_all = jnp.sum(jnp.where(picks, gate_live[:, :, None], jnp.float32(0.0)), axis=1)
    combine_all = combine_all.reshape(row_count, tok_total, local_slots, DEPTH)
    expert_sum = jnp.zeros((row_count, width), jnp.float32)
    for local in range(local_slots):
        rows_in = arrived[:, local].reshape(tok_total * DEPTH, width)
        hidden = jnp.dot(rows_in, w_in[local], preferred_element_type=jnp.float32)
        activated = (
            jax.nn.silu(hidden[:, :hidden_units]) * hidden[:, hidden_units:]
        ).astype(jnp.bfloat16)
        computed = jnp.dot(activated, w_out[local], preferred_element_type=jnp.float32).astype(
            jnp.bfloat16
        )
        computed = computed.reshape(tok_total, DEPTH, width)
        arrived, computed = lax.optimization_barrier((arrived, computed))
        returned = lax.all_to_all(computed, "tok", split_axis=0, concat_axis=0, tiled=True)
        returned = returned.reshape(tok_total * DEPTH, width)
        combine = combine_all[:, :, local].reshape(row_count, tok_total * DEPTH)
        expert_sum = expert_sum + jnp.dot(
            combine.astype(jnp.bfloat16), returned, preferred_element_type=jnp.float32
        )
    stream_out = (stream.astype(jnp.float32) + expert_sum).astype(jnp.bfloat16)
    next_normed = rms_norm(stream_out, gain_next)
    return (stream_out, next_normed)


def solution(mesh):
    return jax.shard_map(
        shards,
        mesh=mesh,
        in_specs=(
            P("tok", "tp"),
            P("tp", None),
            P(("tok", "tp"), None),
            P(),
            P(),
            P(("tok", "tp"), None),
            P(),
            P(),
            P("tok", None, None),
            P("tok", None, None),
            P(),
        ),
        out_specs=(P(("tok", "tp"), None), P(("tok", "tp"), None)),
        check_vma=False,
    )
```
